32 devices in a mesh: groups: 2 (over x), section: 16 (over z, y, core).
Axes of the slice: x: 2, y: 2, z: 4, core: 2. Of those that a mesh axis runs over, the one named last changes fastest.
Arguments:
- section_input: bfloat16 [32, 128, 4096], P(('groups', 'section')), parts along dimension 0, may hold values from -6 to 6
- stash: bfloat16 [32, 128, 4096], P(('groups', 'section')), parts along dimension 0, may hold values from -6 to 6
- cotangent: bfloat16 [32, 128, 4096], P(('groups', 'section')), parts along dimension 0, may hold values from -6 to 6
- norm_gain: float32 [16, 4096], P('section'), may hold values from 0.1 to 1.9
- w_query: bfloat16 [16, 4096, 256], P('section'), may hold values from -0.09375 to 0.09375
- w_kv: bfloat16 [16, 4096, 256], P('section'), may hold values from -0.09375 to 0.09375
- w_out: bfloat16 [16, 256, 4096], P('section'), may hold values from -0.375 to 0.375
- doc_ids: int32 [32, 2, 128], P(('groups', 'section')), parts along dimension 0, may hold values from 0 to 7, never falling along the last dimension, each value on 1 to 64 neighbouring positions
Outputs:
- forwarded: bfloat16 [32, 128, 4096], P(('groups', 'section')), parts along dimension 0
- returned: bfloat16 [32, 128, 4096], P(('groups', 'section')), parts along dimension 0
The draws below stay inside these ranges and needn't reach their ends.
There are 2 independent parts, one for each index of `groups`. The reference program is written for one: setup_inputs(seed, part) draws one part's arguments, and reference() takes and returns one part's arrays. A program takes and returns all parts, laid end to end along the dimension named above; an argument that names none is the same for every part. Nothing has to cross between parts.
Inputs may be any that keep to these rules, and one draw needn't show every extreme that they name: `doc_ids`: ids never fall along a row; each document holds 1 to 64 tokens and one holds exactly that many.
All inputs are finite; a program needn't handle non-finite values.
Results may differ from the reference program's by a relative error of at most 0.01.
Values may be sent and summed in bfloat16 or wider, within the bound.
No kernel may reach another device: no remote copies, remote signals or barrier semaphores. Data moves between devices by JAX's collectives and lax.ppermute only.
A program may use at most 64 MiB of HBM per device.

```python
import math
import jax
import jax.numpy as jnp
import numpy as np
from jax import lax

D = 4096
HEAD_DIM = 128
QHEADS = 2
TOK_MB = 128
SECTIONS = 16


def block_scale(stream_key, shape, split, least, largest):
    def one(dim, parts):
        draws = jax.random.uniform(jax.random.fold_in(jax.random.fold_in(stream_key, 6), dim), (parts,), jnp.float32, least / len(split), largest / len(split))
        return jnp.repeat(jnp.exp(draws), shape[dim] // parts).reshape((-1,) + (1,) * (len(shape) - dim - 1))

    level = one(*split[0])
    for cut in split[1:]:
        level = level * one(*cut)
    return level


def split_up(count, total, most, lean):
    loads = [(1 << 20) // math.isqrt(rank ** lean) + 1 for rank in range(2, count + 1)]
    spare, given = total - most - (count - 1), [1] * (count - 1)
    while spare > 0:
        candidates = [i for i in range(count - 1) if given[i] < most]
        whole, budget = sum([loads[i] for i in candidates]), spare
        for i in candidates:
            more = min(most - given[i], max(1, budget * loads[i] // whole), spare)
            given[i] = given[i] + more
            spare = spare - more
    return np.array([most] + given)


def ragged_sizes(stream_key, number_of, total, reach, lean):
    if number_of == 2:
        one = jax.random.randint(stream_key, (), max(1, total - reach), min(reach, total - 1) + 1)
        return jnp.stack([one, total - one])
    sizes = jnp.asarray(split_up(number_of, total, reach, lean), jnp.int32)
    couples = (number_of - 1) // 2
    source_of, taker = sizes[1:1 + 2 * couples:2], sizes[2:2 + 2 * couples:2]
    slack = jnp.minimum(source_of - 1, reach - taker)
    moved = jax.random.randint(jax.random.fold_in(stream_key, 1), (couples,), 0, 1 << 20) % (slack + 1)
    sizes = sizes.at[1:1 + 2 * couples:2].set(source_of - moved).at[2:2 + 2 * couples:2].set(taker + moved)
    return sizes[jax.random.permutation(jax.random.fold_in(stream_key, 2), number_of)]


def scatter_about(own_key, extent, width, limit, split=(), held_as=jnp.bfloat16):
    loudness = block_scale(own_key, extent, split, -0.22, 0.18) if split else 1.0
    drawn = jax.random.normal(own_key, extent, jnp.float32) * width * loudness
    return jnp.minimum(jnp.maximum(drawn, -limit), limit).astype(held_as)


def setup_inputs(seed: int = 0, part: int = 0) -> dict:
    seeds = jax.random.split(jax.random.key(seed), 9)
    part_keys = jax.random.split(jax.random.fold_in(seeds[8], part), 9)
    section_input = scatter_about(part_keys[0], (SECTIONS, TOK_MB, D), 1.0, 6.0, ((0, 16),))
    stash = scatter_about(part_keys[1], (SECTIONS, TOK_MB, D), 1.0, 6.0, ((0, 16),))
    cotangent = scatter_about(part_keys[2], (SECTIONS, TOK_MB, D), 1.0, 6.0, ((0, 16),))
    norm_gain = jnp.clip(1.0 + 0.18 * jax.random.normal(seeds[3], (SECTIONS, D), jnp.float32), 0.1, 1.9)
    w_query = scatter_about(seeds[4], (SECTIONS, D, QHEADS * HEAD_DIM), D ** -0.5, 0.09375, ((0, 16),))
    w_kv = scatter_about(seeds[5], (SECTIONS, D, 2 * HEAD_DIM), D ** -0.5, 0.09375, ((0, 16),))
    w_out = scatter_about(seeds[6], (SECTIONS, QHEADS * HEAD_DIM, D), (QHEADS * HEAD_DIM) ** -0.5, 0.375, ((0, 16),))
    doc_ids = jax.vmap(lambda own: jnp.searchsorted(jnp.cumsum(ragged_sizes(own, TOK_MB // 16, TOK_MB, TOK_MB // 2, 2)), jnp.arange(TOK_MB), side="right"))(jax.random.split(part_keys[7], SECTIONS * 2)).reshape((SECTIONS, 2, TOK_MB)).astype(jnp.int32)
    return dict(section_input=section_input, stash=stash, cotangent=cotangent, norm_gain=norm_gain, w_query=w_query, w_kv=w_kv, w_out=w_out, doc_ids=doc_ids)


def rotary_tables(segment, head_dim):
    index = jnp.arange(segment.shape[0], dtype=jnp.int32)
    first = jnp.concatenate([jnp.ones((1,), dtype=bool), segment[1:] != segment[:-1]])
    starts = jnp.where(first, index, jnp.zeros_like(index))
    places = (index - lax.cummax(starts, axis=0)).astype(jnp.float32)
    half = head_dim // 2
    freqs = 500000.0 ** (-(jnp.arange(half, dtype=jnp.float32) * 2.0 / head_dim))
    angles = places[:, None] * freqs[None, :]
    cosine = jnp.concatenate([jnp.cos(angles), jnp.cos(angles)], -1)
    sine_part = jnp.concatenate([jnp.sin(angles), jnp.sin(angles)], -1)
    return (cosine, sine_part)

def rotary(block, cosine, sine_part):
    half = block.shape[-1] // 2
    turned = jnp.concatenate([-block[..., half:], block[..., :half]], -1)
    return block * cosine + turned * sine_part

def section_layer(acts, gain, w_query, w_kv, w_out, segment):
    rows = acts.shape[0]
    head_dim = w_kv.shape[1] // 2
    heads = w_query.shape[1] // head_dim
    values32 = acts.astype(jnp.float32)
    scale = lax.rsqrt(lax.optimization_barrier(jnp.mean(values32 * values32, axis=-1, keepdims=True)) + 1e-05)
    normed = (values32 * scale * gain).astype(jnp.bfloat16)
    query = jnp.dot(normed, w_query, preferred_element_type=jnp.float32).reshape(rows, heads, head_dim)
    keyval = jnp.dot(normed, w_kv, preferred_element_type=jnp.float32)
    cosine, sine_part = rotary_tables(segment, head_dim)
    query = rotary(query, cosine[:, None, :], sine_part[:, None, :]).astype(jnp.bfloat16)
    keys = rotary(keyval[:, :head_dim], cosine, sine_part).astype(jnp.bfloat16)
    values = keyval[:, head_dim:].astype(jnp.bfloat16)
    scores = jnp.einsum('qhd,kd->hqk', query.astype(jnp.float32), keys.astype(jnp.float32)) / math.sqrt(head_dim)
    index = jnp.arange(rows, dtype=jnp.int32)
    allowed = (segment[:, None] == segment[None, :]) & (index[None, :] <= index[:, None])
    expd = jnp.where(allowed[None], jnp.exp(scores), jnp.zeros_like(scores))
    probs = (expd / lax.optimization_barrier(jnp.sum(expd, axis=-1, keepdims=True))).astype(jnp.bfloat16)
    mixed = jnp.einsum('hqk,kd->qhd', probs.astype(jnp.float32), values.astype(jnp.float32))
    mixed = mixed.astype(jnp.bfloat16).reshape(rows, heads * head_dim)
    return (values32 + jnp.dot(mixed, w_out, preferred_element_type=jnp.float32)).astype(jnp.bfloat16)

def reference(section_input, stash, cotangent, norm_gain, w_query, w_kv, w_out, doc_ids):

    def one_section(section):
        outward = section_layer(section_input[section], norm_gain[section], w_query[section], w_kv[section], w_out[section], doc_ids[section, 0])
        saved = stash[SECTIONS - 1 - section]

        def replay(acts):
            return section_layer(acts, norm_gain[section], w_query[section], w_kv[section], w_out[section], doc_ids[section, 1])
        unused, pullback = jax.vjp(replay, saved)
        return (outward, pullback(cotangent[section])[0])
    outs_fwd, outs_grad = lax.map(one_section, jnp.arange(SECTIONS, dtype=jnp.int32))
    blank = jnp.zeros((1,) + outs_fwd.shape[1:], outs_fwd.dtype)
    forwarded = jnp.concatenate([blank, outs_fwd[:-1]], 0)
    returned = jnp.concatenate([outs_grad[1:], blank], 0)
    return (forwarded, returned)
```

```python
import math

import jax
import jax.numpy as jnp
from jax import lax
from jax.sharding import PartitionSpec as P


def shifted(value, axis, steps):
    count = lax.axis_size(axis)
    leading, last = (max(0, -steps), min(count, count - steps))
    return lax.ppermute(value, axis, [(source, source + steps) for source in range(leading, last)])


def rotary_tables(segment, head_dim):
    index = jnp.arange(segment.shape[0], dtype=jnp.int32)
    first = jnp.concatenate([jnp.ones((1,), dtype=bool), segment[1:] != segment[:-1]])
    starts = jnp.where(first, index, jnp.zeros_like(index))
    places = (index - lax.cummax(starts, axis=0)).astype(jnp.float32)
    half = head_dim // 2
    freqs = 500000.0 ** (-(jnp.arange(half, dtype=jnp.float32) * 2.0 / head_dim))
    angles = places[:, None] * freqs[None, :]
    cosine = jnp.concatenate([jnp.cos(angles), jnp.cos(angles)], -1)
    sine_part = jnp.concatenate([jnp.sin(angles), jnp.sin(angles)], -1)
    return (cosine, sine_part)


def rotary(block, cosine, sine_part):
    half = block.shape[-1] // 2
    turned = jnp.concatenate([-block[..., half:], block[..., :half]], -1)
    return block * cosine + turned * sine_part


def section_layer(acts, gain, w_query, w_kv, w_out, segment):
    rows = acts.shape[0]
    head_dim = w_kv.shape[1] // 2
    heads = w_query.shape[1] // head_dim
    values32 = acts.astype(jnp.float32)
    scale = lax.rsqrt(jnp.mean(values32 * values32, axis=-1, keepdims=True) + 1e-05)
    normed = (values32 * scale * gain).astype(jnp.bfloat16)
    query = jnp.dot(normed, w_query, preferred_element_type=jnp.float32).reshape(
        rows, heads, head_dim
    )
    keyval = jnp.dot(normed, w_kv, preferred_element_type=jnp.float32)
    cosine, sine_part = rotary_tables(segment, head_dim)
    query = rotary(query, cosine[:, None, :], sine_part[:, None, :]).astype(jnp.bfloat16)
    keys = rotary(keyval[:, :head_dim], cosine, sine_part).astype(jnp.bfloat16)
    values = keyval[:, head_dim:].astype(jnp.bfloat16)
    scores = jnp.einsum("qhd,kd->hqk", query, keys, preferred_element_type=jnp.float32) / math.sqrt(
        head_dim
    )
    index = jnp.arange(rows, dtype=jnp.int32)
    allowed = (segment[:, None] == segment[None, :]) & (index[None, :] <= index[:, None])
    expd = jnp.where(allowed[None], jnp.exp(scores), jnp.zeros_like(scores))
    probs = (expd / jnp.sum(expd, axis=-1, keepdims=True)).astype(jnp.bfloat16)
    mixed = jnp.einsum("hqk,kd->qhd", probs, values, preferred_element_type=jnp.float32)
    mixed = mixed.astype(jnp.bfloat16).reshape(rows, heads * head_dim)
    return (values32 + jnp.dot(mixed, w_out, preferred_element_type=jnp.float32)).astype(
        jnp.bfloat16
    )


def shards(section_input, stash, cotangent, norm_gain, w_query, w_kv, w_out, doc_ids):
    pieces = lax.axis_size("section")
    mirror = [(source, pieces - 1 - source) for source in range(pieces)]
    fetched = lax.ppermute(stash[0], "section", mirror)
    outward = section_layer(
        section_input[0], norm_gain[0], w_query[0], w_kv[0], w_out[0], doc_ids[0, 0]
    )

    def replay(acts):
        return section_layer(acts, norm_gain[0], w_query[0], w_kv[0], w_out[0], doc_ids[0, 1])

    unused, pullback = jax.vjp(replay, fetched)
    gradient = pullback(cotangent[0])[0]
    forwarded = shifted(outward[None], "section", 1)
    returned = shifted(gradient[None], "section", -1)
    return (forwarded, returned)


def solution(mesh):
    return jax.shard_map(
        shards,
        mesh=mesh,
        in_specs=(
            P(("groups", "section"), None, None),
            P(("groups", "section"), None, None),
            P(("groups", "section"), None, None),
            P("section", None),
            P("section", None, None),
            P("section", None, None),
            P("section", None, None),
            P(("groups", "section"), None, None),
        ),
        out_specs=(P(("groups", "section"), None, None), P(("groups", "section"), None, None)),
        check_vma=False,
    )
```

```python
import math

import jax
import jax.numpy as jnp
from jax import lax
from jax.sharding import PartitionSpec as P


def shifted(value, axis, steps):
    count = lax.axis_size(axis)
    leading, last = (max(0, -steps), min(count, count - steps))
    return lax.ppermute(value, axis, [(source, source + steps) for source in range(leading, last)])


def rotary_tables(segment, head_dim):
    index = jnp.arange(segment.shape[0], dtype=jnp.int32)
    first = jnp.concatenate([jnp.ones((1,), dtype=bool), segment[1:] != segment[:-1]])
    starts = jnp.where(first, index, jnp.zeros_like(index))
    places = (index - lax.cummax(starts, axis=0)).astype(jnp.float32)
    half = head_dim // 2
    freqs = 500000.0 ** (-(jnp.arange(half, dtype=jnp.float32) * 2.0 / head_dim))
    angles = places[:, None] * freqs[None, :]
    cosine = jnp.concatenate([jnp.cos(angles), jnp.cos(angles)], -1)
    sine_part = jnp.concatenate([jnp.sin(angles), jnp.sin(angles)], -1)
    return (cosine, sine_part)


def rotary(block, cosine, sine_part):
    half = block.shape[-1] // 2
    turned = jnp.concatenate([-block[..., half:], block[..., :half]], -1)
    return block * cosine + turned * sine_part


def section_layer(acts, gain, w_query, w_kv, w_out, segment):
    rows = acts.shape[0]
    head_dim = w_kv.shape[1] // 2
    heads = w_query.shape[1] // head_dim
    values32 = acts.astype(jnp.float32)
    scale = lax.rsqrt(jnp.mean(values32 * values32, axis=-1, keepdims=True) + 1e-05)
    normed = (values32 * scale * gain).astype(jnp.bfloat16)
    query = jnp.dot(normed, w_query, preferred_element_type=jnp.float32).reshape(
        rows, heads, head_dim
    )
    keyval = jnp.dot(normed, w_kv, preferred_element_type=jnp.float32)
    cosine, sine_part = rotary_tables(segment, head_dim)
    query = rotary(query, cosine[:, None, :], sine_part[:, None, :]).astype(jnp.bfloat16)
    keys = rotary(keyval[:, :head_dim], cosine, sine_part).astype(jnp.bfloat16)
    values = keyval[:, head_dim:].astype(jnp.bfloat16)
    scores = jnp.einsum("qhd,kd->hqk", query, keys, preferred_element_type=jnp.float32) / math.sqrt(
        head_dim
    )
    index = jnp.arange(rows, dtype=jnp.int32)
    allowed = (segment[:, None] == segment[None, :]) & (index[None, :] <= index[:, None])
    expd = jnp.where(allowed[None], jnp.exp(scores), jnp.zeros_like(scores))
    probs = (expd / jnp.sum(expd, axis=-1, keepdims=True)).astype(jnp.bfloat16)
    mixed = jnp.einsum("hqk,kd->qhd", probs, values, preferred_element_type=jnp.float32)
    mixed = mixed.astype(jnp.bfloat16).reshape(rows, heads * head_dim)
    return (values32 + jnp.dot(mixed, w_out, preferred_element_type=jnp.float32)).astype(
        jnp.bfloat16
    )


def shards(section_input, stash, cotangent, norm_gain, w_query, w_kv, w_out, doc_ids):
    pieces = lax.axis_size("section")
    mirror = [(source, pieces - 1 - source) for source in range(pieces)]
    rows = stash.shape[1]
    chunks = 4 if rows % 32 == 0 else 1
    step = rows // chunks
    fetched = jnp.concatenate(
        [
            lax.ppermute(stash[0, start : start + step], "section", mirror)
            for start in range(0, rows, step)
        ],
        0,
    )
    outward = section_layer(
        section_input[0], norm_gain[0], w_query[0], w_kv[0], w_out[0], doc_ids[0, 0]
    )

    def replay(acts):
        return section_layer(acts, norm_gain[0], w_query[0], w_kv[0], w_out[0], doc_ids[0, 1])

    unused, pullback = jax.vjp(replay, fetched)
    gradient = pullback(cotangent[0])[0]
    forwarded = shifted(outward[None], "section", 1)
    returned = shifted(gradient[None], "section", -1)
    return (forwarded, returned)


def solution(mesh):
    return jax.shard_map(
        shards,
        mesh=mesh,
        in_specs=(
            P(("groups", "section"), None, None),
            P(("groups", "section"), None, None),
            P(("groups", "section"), None, None),
            P("section", None),
            P("section", None, None),
            P("section", None, None),
            P("section", None, None),
            P(("groups", "section"), None, None),
        ),
        out_specs=(P(("groups", "section"), None, None), P(("groups", "section"), None, None)),
        check_vma=False,
    )
```

```python
import math

import jax
import jax.numpy as jnp
from jax import lax
from jax.sharding import PartitionSpec as P


def shifted(value, axis, steps):
    count = lax.axis_size(axis)
    leading, last = (max(0, -steps), min(count, count - steps))
    return lax.ppermute(value, axis, [(source, source + steps) for source in range(leading, last)])


def rotary_tables(segment, head_dim):
    index = jnp.arange(segment.shape[0], dtype=jnp.int32)
    first = jnp.concatenate([jnp.ones((1,), dtype=bool), segment[1:] != segment[:-1]])
    starts = jnp.where(first, index, jnp.zeros_like(index))
    places = (index - lax.cummax(starts, axis=0)).astype(jnp.float32)
    half = head_dim // 2
    freqs = 500000.0 ** (-(jnp.arange(half, dtype=jnp.float32) * 2.0 / head_dim))
    angles = places[:, None] * freqs[None, :]
    cosine = jnp.concatenate([jnp.cos(angles), jnp.cos(angles)], -1)
    sine_part = jnp.concatenate([jnp.sin(angles), jnp.sin(angles)], -1)
    return (cosine, sine_part)


def rotary(block, cosine, sine_part):
    half = block.shape[-1] // 2
    turned = jnp.concatenate([-block[..., half:], block[..., :half]], -1)
    return block * cosine + turned * sine_part


def section_layer(acts, gain, w_query, w_kv, w_out, segment):
    rows = acts.shape[0]
    head_dim = w_kv.shape[1] // 2
    heads = w_query.shape[1] // head_dim
    values32 = acts.astype(jnp.float32)
    scale = lax.rsqrt(jnp.mean(values32 * values32, axis=-1, keepdims=True) + 1e-05)
    normed = (values32 * scale * gain).astype(jnp.bfloat16)
    query = jnp.dot(normed, w_query, preferred_element_type=jnp.float32)
    keyval = jnp.dot(normed, w_kv, preferred_element_type=jnp.float32)
    cosine, sine_part = rotary_tables(segment, head_dim)
    keys = rotary(keyval[:, :head_dim], cosine, sine_part).astype(jnp.bfloat16)
    values = keyval[:, head_dim:].astype(jnp.bfloat16)
    index = jnp.arange(rows, dtype=jnp.int32)
    allowed = (segment[:, None] == segment[None, :]) & (index[None, :] <= index[:, None])
    mixed = []
    for head in range(heads):
        part = query[:, head * head_dim : (head + 1) * head_dim]
        part = rotary(part, cosine, sine_part).astype(jnp.bfloat16)
        scores = lax.dot_general(
            part, keys, (((1,), (1,)), ((), ())), preferred_element_type=jnp.float32
        ) / math.sqrt(head_dim)
        expd = jnp.where(allowed, jnp.exp(scores), jnp.zeros_like(scores))
        probs = (expd / jnp.sum(expd, axis=-1, keepdims=True)).astype(jnp.bfloat16)
        mixed.append(
            jnp.dot(probs, values, preferred_element_type=jnp.float32).astype(jnp.bfloat16)
        )
    mixed = jnp.concatenate(mixed, -1)
    return (values32 + jnp.dot(mixed, w_out, preferred_element_type=jnp.float32)).astype(
        jnp.bfloat16
    )


def shards(section_input, stash, cotangent, norm_gain, w_query, w_kv, w_out, doc_ids):
    pieces = lax.axis_size("section")
    mirror = [(source, pieces - 1 - source) for source in range(pieces)]
    fetched = lax.ppermute(stash[0], "section", mirror)
    outward = section_layer(
        section_input[0], norm_gain[0], w_query[0], w_kv[0], w_out[0], doc_ids[0, 0]
    )

    def replay(acts):
        return section_layer(acts, norm_gain[0], w_query[0], w_kv[0], w_out[0], doc_ids[0, 1])

    unused, pullback = jax.vjp(replay, fetched)
    gradient = pullback(cotangent[0])[0]
    forwarded = shifted(outward[None], "section", 1)
    returned = shifted(gradient[None], "section", -1)
    return (forwarded, returned)


def solution(mesh):
    return jax.shard_map(
        shards,
        mesh=mesh,
        in_specs=(
            P(("groups", "section"), None, None),
            P(("groups", "section"), None, None),
            P(("groups", "section"), None, None),
            P("section", None),
            P("section", None, None),
            P("section", None, None),
            P("section", None, None),
            P(("groups", "section"), None, None),
        ),
        out_specs=(P(("groups", "section"), None, None), P(("groups", "section"), None, None)),
        check_vma=False,
    )
```

```python
import math

import jax
import jax.numpy as jnp
from jax import lax
from jax.sharding import PartitionSpec as P


def shifted(value, axis, steps):
    count = lax.axis_size(axis)
    leading, last = (max(0, -steps), min(count, count - steps))
    return lax.ppermute(value, axis, [(source, source + steps) for source in range(leading, last)])


def rotary_tables(segment, head_dim):
    index = jnp.arange(segment.shape[0], dtype=jnp.int32)
    first = jnp.concatenate([jnp.ones((1,), dtype=bool), segment[1:] != segment[:-1]])
    starts = jnp.where(first, index, jnp.zeros_like(index))
    places = (index - lax.cummax(starts, axis=0)).astype(jnp.float32)
    half = head_dim // 2
    freqs = 500000.0 ** (-(jnp.arange(half, dtype=jnp.float32) * 2.0 / head_dim))
    angles = places[:, None] * freqs[None, :]
    cosine = jnp.concatenate([jnp.cos(angles), jnp.cos(angles)], -1)
    sine_part = jnp.concatenate([jnp.sin(angles), jnp.sin(angles)], -1)
    return (cosine, sine_part)


def rotary(block, cosine, sine_part):
    half = block.shape[-1] // 2
    turned = jnp.concatenate([-block[..., half:], block[..., :half]], -1)
    return block * cosine + turned * sine_part


def section_layer(acts, gain, w_query, w_kv, w_out, segment):
    rows = acts.shape[0]
    head_dim = w_kv.shape[1] // 2
    heads = w_query.shape[1] // head_dim
    values32 = acts.astype(jnp.float32)
    scale = lax.rsqrt(jnp.mean(values32 * values32, axis=-1, keepdims=True) + 1e-05)
    normed = (values32 * scale * gain).astype(jnp.bfloat16)
    query = jnp.dot(normed, w_query, preferred_element_type=jnp.float32)
    keyval = jnp.dot(normed, w_kv, preferred_element_type=jnp.float32)
    cosine, sine_part = rotary_tables(segment, head_dim)
    keys = rotary(keyval[:, :head_dim], cosine, sine_part).astype(jnp.bfloat16)
    values = keyval[:, head_dim:].astype(jnp.bfloat16)
    index = jnp.arange(rows, dtype=jnp.int32)
    allowed = (segment[:, None] == segment[None, :]) & (index[None, :] <= index[:, None])
    mixed = []
    for head in range(heads):
        part = query[:, head * head_dim : (head + 1) * head_dim]
        part = rotary(part, cosine, sine_part).astype(jnp.bfloat16)
        scores = lax.dot_general(
            part, keys, (((1,), (1,)), ((), ())), preferred_element_type=jnp.float32
        ) / math.sqrt(head_dim)
        expd = jnp.where(allowed, jnp.exp(scores), jnp.zeros_like(scores))
        probs = (expd / jnp.sum(expd, axis=-1, keepdims=True)).astype(jnp.bfloat16)
        mixed.append(
            jnp.dot(probs, values, preferred_element_type=jnp.float32).astype(jnp.bfloat16)
        )
    mixed = jnp.concatenate(mixed, -1)
    return (values32 + jnp.dot(mixed, w_out, preferred_element_type=jnp.float32)).astype(
        jnp.bfloat16
    )


def shards(section_input, stash, cotangent, norm_gain, w_query, w_kv, w_out, doc_ids):
    pieces = lax.axis_size("section")
    mirror = [(source, pieces - 1 - source) for source in range(pieces)]
    fetched = lax.ppermute(stash[0], "section", mirror)
    outward = section_layer(
        section_input[0], norm_gain[0], w_query[0], w_kv[0], w_out[0], doc_ids[0, 0]
    )

    def replay(acts):
        return section_layer(acts, norm_gain[0], w_query[0], w_kv[0], w_out[0], doc_ids[0, 1])

    unused, pullback = jax.vjp(replay, fetched)
    gradient = pullback(cotangent[0])[0]
    forwarded = shifted(outward[None], "section", 1)
    half = gradient.shape[0] // 2
    returned = jnp.concatenate(
        [shifted(gradient[None, :half], "section", -1), shifted(gradient[None, half:], "section", -1)],
        1,
    )
    return (forwarded, returned)


def solution(mesh):
    return jax.shard_map(
        shards,
        mesh=mesh,
        in_specs=(
            P(("groups", "section"), None, None),
            P(("groups", "section"), None, None),
            P(("groups", "section"), None, None),
            P("section", None),
            P("section", None, None),
            P("section", None, None),
            P("section", None, None),
            P(("groups", "section"), None, None),
        ),
        out_specs=(P(("groups", "section"), None, None), P(("groups", "section"), None, None)),
        check_vma=False,
    )
```

```python
import math

import jax
import jax.numpy as jnp
from jax import lax
from jax.sharding import PartitionSpec as P


def shifted(value, axis, steps):
    count = lax.axis_size(axis)
    leading, last = (max(0, -steps), min(count, count - steps))
    return lax.ppermute(value, axis, [(source, source + steps) for source in range(leading, last)])


def rotary_tables(segment, head_dim):
    index = jnp.arange(segment.shape[0], dtype=jnp.int32)
    first = jnp.concatenate([jnp.ones((1,), dtype=bool), segment[1:] != segment[:-1]])
    starts = jnp.where(first, index, jnp.zeros_like(index))
    places = (index - lax.cummax(starts, axis=0)).astype(jnp.float32)
    half = head_dim // 2
    freqs = 500000.0 ** (-(jnp.arange(half, dtype=jnp.float32) * 2.0 / head_dim))
    angles = places[:, None] * freqs[None, :]
    cosine = jnp.concatenate([jnp.cos(angles), jnp.cos(angles)], -1)
    sine_part = jnp.concatenate([jnp.sin(angles), jnp.sin(angles)], -1)
    return (cosine, sine_part)


def rotary(block, cosine, sine_part):
    half = block.shape[-1] // 2
    turned = jnp.concatenate([-block[..., half:], block[..., :half]], -1)
    return block * cosine + turned * sine_part


def section_layer(acts, gain, w_query, w_kv, w_out, segment):
    rows = acts.shape[0]
    head_dim = w_kv.shape[1] // 2
    heads = w_query.shape[1] // head_dim
    values32 = acts.astype(jnp.float32)
    scale = lax.rsqrt(jnp.mean(values32 * values32, axis=-1, keepdims=True) + 1e-05)
    normed = (values32 * scale * gain).astype(jnp.bfloat16)
    query = jnp.dot(normed, w_query, preferred_element_type=jnp.float32)
    keyval = jnp.dot(normed, w_kv, preferred_element_type=jnp.float32)
    cosine, sine_part = rotary_tables(segment, head_dim)
    keys = rotary(keyval[:, :head_dim], cosine, sine_part).astype(jnp.bfloat16)
    values = keyval[:, head_dim:].astype(jnp.bfloat16)
    index = jnp.arange(rows, dtype=jnp.int32)
    allowed = (segment[:, None] == segment[None, :]) & (index[None, :] <= index[:, None])
    mixed = []
    for head in range(heads):
        part = query[:, head * head_dim : (head + 1) * head_dim]
        part = rotary(part, cosine, sine_part).astype(jnp.bfloat16)
        scores = lax.dot_general(
            part, keys, (((1,), (1,)), ((), ())), preferred_element_type=jnp.float32
        ) / math.sqrt(head_dim)
        expd = jnp.where(allowed, jnp.exp(scores), jnp.zeros_like(scores))
        probs = (expd / jnp.sum(expd, axis=-1, keepdims=True)).astype(jnp.bfloat16)
        mixed.append(
            jnp.dot(probs, values, preferred_element_type=jnp.float32).astype(jnp.bfloat16)
        )
    mixed = jnp.concatenate(mixed, -1)
    return (values32 + jnp.dot(mixed, w_out, preferred_element_type=jnp.float32)).astype(
        jnp.bfloat16
    )


def shards(section_input, stash, cotangent, norm_gain, w_query, w_kv, w_out, doc_ids):
    pieces = lax.axis_size("section")
    mirror = [(source, pieces - 1 - source) for source in range(pieces)]
    fetched = lax.ppermute(stash[0], "section", mirror)
    outward = section_layer(
        section_input[0], norm_gain[0], w_query[0], w_kv[0], w_out[0], doc_ids[0, 0]
    )

    def replay(acts):
        return section_layer(acts, norm_gain[0], w_query[0], w_kv[0], w_out[0], doc_ids[0, 1])

    outward, fetched = lax.optimization_barrier((outward, fetched))
    unused, pullback = jax.vjp(replay, fetched)
    gradient = pullback(cotangent[0])[0]
    forwarded = shifted(outward[None], "section", 1)
    returned = shifted(gradient[None], "section", -1)
    return (forwarded, returned)


def solution(mesh):
    return jax.shard_map(
        shards,
        mesh=mesh,
        in_specs=(
            P(("groups", "section"), None, None),
            P(("groups", "section"), None, None),
            P(("groups", "section"), None, None),
            P("section", None),
            P("section", None, None),
            P("section", None, None),
            P("section", None, None),
            P(("groups", "section"), None, None),
        ),
        out_specs=(P(("groups", "section"), None, None), P(("groups", "section"), None, None)),
        check_vma=False,
    )
```

```python
import math

import jax
import jax.numpy as jnp
from jax import lax
from jax.sharding import PartitionSpec as P


def shifted(value, axis, steps):
    count = lax.axis_size(axis)
    leading, last = (max(0, -steps), min(count, count - steps))
    return lax.ppermute(value, axis, [(source, source + steps) for source in range(leading, last)])


def rotary_tables(segment, head_dim):
    index = jnp.arange(segment.shape[0], dtype=jnp.int32)
    first = jnp.concatenate([jnp.ones((1,), dtype=bool), segment[1:] != segment[:-1]])
    starts = jnp.where(first, index, jnp.zeros_like(index))
    places = (index - lax.cummax(starts, axis=0)).astype(jnp.float32)
    half = head_dim // 2
    freqs = 500000.0 ** (-(jnp.arange(half, dtype=jnp.float32) * 2.0 / head_dim))
    angles = places[:, None] * freqs[None, :]
    cosine = jnp.concatenate([jnp.cos(angles), jnp.cos(angles)], -1)
    sine_part = jnp.concatenate([jnp.sin(angles), jnp.sin(angles)], -1)
    return (cosine, sine_part)


def rotary(block, cosine, sine_part):
    half = block.shape[-1] // 2
    turned = jnp.concatenate([-block[..., half:], block[..., :half]], -1)
    return block * cosine + turned * sine_part


def section_layer(acts, gain, w_query, w_kv, w_out, segment):
    rows = acts.shape[0]
    head_dim = w_kv.shape[1] // 2
    heads = w_query.shape[1] // head_dim
    values32 = acts.astype(jnp.float32)
    scale = lax.rsqrt(jnp.mean(values32 * values32, axis=-1, keepdims=True) + 1e-05)
    normed = (values32 * scale * gain).astype(jnp.bfloat16)
    query = jnp.dot(normed, w_query, preferred_element_type=jnp.float32)
    keyval = jnp.dot(normed, w_kv, preferred_element_type=jnp.float32)
    cosine, sine_part = rotary_tables(segment, head_dim)
    keys = rotary(keyval[:, :head_dim], cosine, sine_part).astype(jnp.bfloat16)
    values = keyval[:, head_dim:].astype(jnp.bfloat16)
    index = jnp.arange(rows, dtype=jnp.int32)
    allowed = (segment[:, None] == segment[None, :]) & (index[None, :] <= index[:, None])
    mixed = []
    for head in range(heads):
        part = query[:, head * head_dim : (head + 1) * head_dim]
        part = rotary(part, cosine, sine_part).astype(jnp.bfloat16)
        scores = lax.dot_general(
            part, keys, (((1,), (1,)), ((), ())), preferred_element_type=jnp.float32
        ) / math.sqrt(head_dim)
        expd = jnp.where(allowed, jnp.exp(scores), jnp.zeros_like(scores))
        probs = (expd / jnp.sum(expd, axis=-1, keepdims=True)).astype(jnp.bfloat16)
        mixed.append(
            jnp.dot(probs, values, preferred_element_type=jnp.float32).astype(jnp.bfloat16)
        )
    mixed = jnp.concatenate(mixed, -1)
    return (values32 + jnp.dot(mixed, w_out, preferred_element_type=jnp.float32)).astype(
        jnp.bfloat16
    )


def shards(section_input, stash, cotangent, norm_gain, w_query, w_kv, w_out, doc_ids):
    pieces = lax.axis_size("section")
    mirror = [(source, pieces - 1 - source) for source in range(pieces)]
    fetched = lax.ppermute(stash[0], "section", mirror)
    outward = section_layer(
        section_input[0], norm_gain[0], w_query[0], w_kv[0], w_out[0], doc_ids[0, 0]
    )

    def replay(acts):
        return section_layer(acts, norm_gain[0], w_query[0], w_kv[0], w_out[0], doc_ids[0, 1])

    cut = pieces // 2 - 1
    early = lax.ppermute(
        outward[None], "section", [(source, source + 1) for source in range(pieces - 1) if source != cut]
    )
    outward, fetched = lax.optimization_barrier((outward, fetched))
    late = lax.ppermute(outward[None], "section", [(cut, cut + 1)])
    forwarded = jnp.where(lax.axis_index("section") == cut + 1, late, early)
    unused, pullback = jax.vjp(replay, fetched)
    gradient = pullback(cotangent[0])[0]
    returned = shifted(gradient[None], "section", -1)
    return (forwarded, returned)


def solution(mesh):
    return jax.shard_map(
        shards,
        mesh=mesh,
        in_specs=(
            P(("groups", "section"), None, None),
            P(("groups", "section"), None, None),
            P(("groups", "section"), None, None),
            P("section", None),
            P("section", None, None),
            P("section", None, None),
            P("section", None, None),
            P(("groups", "section"), None, None),
        ),
        out_specs=(P(("groups", "section"), None, None), P(("groups", "section"), None, None)),
        check_vma=False,
    )
```

```python
import math

import jax
import jax.numpy as jnp
from jax import lax
from jax.sharding import PartitionSpec as P


def shifted(value, axis, steps):
    count = lax.axis_size(axis)
    leading, last = (max(0, -steps), min(count, count - steps))
    return lax.ppermute(value, axis, [(source, source + steps) for source in range(leading, last)])


def rotary_tables(segment, head_dim):
    index = jnp.arange(segment.shape[0], dtype=jnp.int32)
    first = jnp.concatenate([jnp.ones((1,), dtype=bool), segment[1:] != segment[:-1]])
    starts = jnp.where(first, index, jnp.zeros_like(index))
    places = (index - lax.cummax(starts, axis=0)).astype(jnp.float32)
    half = head_dim // 2
    freqs = 500000.0 ** (-(jnp.arange(half, dtype=jnp.float32) * 2.0 / head_dim))
    angles = places[:, None] * freqs[None, :]
    cosine = jnp.concatenate([jnp.cos(angles), jnp.cos(angles)], -1)
    sine_part = jnp.concatenate([jnp.sin(angles), jnp.sin(angles)], -1)
    return (cosine, sine_part)


def rotary(block, cosine, sine_part):
    half = block.shape[-1] // 2
    turned = jnp.concatenate([-block[..., half:], block[..., :half]], -1)
    return block * cosine + turned * sine_part


def section_layer(acts, gain, w_query, w_kv, w_out, segment):
    rows = acts.shape[0]
    head_dim = w_kv.shape[1] // 2
    heads = w_query.shape[1] // head_dim
    values32 = acts.astype(jnp.float32)
    scale = lax.rsqrt(jnp.mean(values32 * values32, axis=-1, keepdims=True) + 1e-05)
    normed = (values32 * scale * gain).astype(jnp.bfloat16)
    query = jnp.dot(normed, w_query, preferred_element_type=jnp.float32)
    keyval = jnp.dot(normed, w_kv, preferred_element_type=jnp.float32)
    cosine, sine_part = rotary_tables(segment, head_dim)
    keys = rotary(keyval[:, :head_dim], cosine, sine_part).astype(jnp.bfloat16)
    values = keyval[:, head_dim:].astype(jnp.bfloat16)
    index = jnp.arange(rows, dtype=jnp.int32)
    allowed = (segment[:, None] == segment[None, :]) & (index[None, :] <= index[:, None])
    stacked = jnp.concatenate(
        [query[:, head * head_dim : (head + 1) * head_dim] for head in range(heads)], 0
    )
    stacked = rotary(
        stacked, jnp.tile(cosine, (heads, 1)), jnp.tile(sine_part, (heads, 1))
    ).astype(jnp.bfloat16)
    scores = lax.dot_general(
        stacked, keys, (((1,), (1,)), ((), ())), preferred_element_type=jnp.float32
    ) / math.sqrt(head_dim)
    expd = jnp.where(jnp.tile(allowed, (heads, 1)), jnp.exp(scores), jnp.zeros_like(scores))
    probs = (expd / jnp.sum(expd, axis=-1, keepdims=True)).astype(jnp.bfloat16)
    mixed = jnp.dot(probs, values, preferred_element_type=jnp.float32).astype(jnp.bfloat16)
    mixed = jnp.concatenate(
        [mixed[head * rows : (head + 1) * rows] for head in range(heads)], -1
    )
    return (values32 + jnp.dot(mixed, w_out, preferred_element_type=jnp.float32)).astype(
        jnp.bfloat16
    )


def shards(section_input, stash, cotangent, norm_gain, w_query, w_kv, w_out, doc_ids):
    pieces = lax.axis_size("section")
    mirror = [(source, pieces - 1 - source) for source in range(pieces)]
    fetched = lax.ppermute(stash[0], "section", mirror)
    outward = section_layer(
        section_input[0], norm_gain[0], w_query[0], w_kv[0], w_out[0], doc_ids[0, 0]
    )

    def replay(acts):
        return section_layer(acts, norm_gain[0], w_query[0], w_kv[0], w_out[0], doc_ids[0, 1])

    unused, pullback = jax.vjp(replay, fetched)
    gradient = pullback(cotangent[0])[0]
    forwarded = shifted(outward[None], "section", 1)
    returned = shifted(gradient[None], "section", -1)
    return (forwarded, returned)


def solution(mesh):
    return jax.shard_map(
        shards,
        mesh=mesh,
        in_specs=(
            P(("groups", "section"), None, None),
            P(("groups", "section"), None, None),
            P(("groups", "section"), None, None),
            P("section", None),
            P("section", None, None),
            P("section", None, None),
            P("section", None, None),
            P(("groups", "section"), None, None),
        ),
        out_specs=(P(("groups", "section"), None, None), P(("groups", "section"), None, None)),
        check_vma=False,
    )
```

```python
import math

import jax
import jax.numpy as jnp
from jax import lax
from jax.sharding import PartitionSpec as P


def shifted(value, axis, steps):
    count = lax.axis_size(axis)
    leading, last = (max(0, -steps), min(count, count - steps))
    return lax.ppermute(value, axis, [(source, source + steps) for source in range(leading, last)])


def rotary_tables(segment, head_dim):
    index = jnp.arange(segment.shape[0], dtype=jnp.int32)
    first = jnp.concatenate([jnp.ones((1,), dtype=bool), segment[1:] != segment[:-1]])
    starts = jnp.where(first, index, jnp.zeros_like(index))
    places = (index - lax.cummax(starts, axis=0)).astype(jnp.float32)
    half = head_dim // 2
    freqs = 500000.0 ** (-(jnp.arange(half, dtype=jnp.float32) * 2.0 / head_dim))
    angles = places[:, None] * freqs[None, :]
    cosine = jnp.concatenate([jnp.cos(angles), jnp.cos(angles)], -1)
    sine_part = jnp.concatenate([jnp.sin(angles), jnp.sin(angles)], -1)
    return (cosine, sine_part)


def rotary(block, cosine, sine_part):
    half = block.shape[-1] // 2
    turned = jnp.concatenate([-block[..., half:], block[..., :half]], -1)
    return block * cosine + turned * sine_part


def section_layer(acts, gain, w_query, w_kv, w_out, segment):
    rows = acts.shape[0]
    head_dim = w_kv.shape[1] // 2
    heads = w_query.shape[1] // head_dim
    values32 = acts.astype(jnp.float32)
    scale = lax.rsqrt(jnp.mean(values32 * values32, axis=-1, keepdims=True) + 1e-05)
    normed = (values32 * scale * gain).astype(jnp.bfloat16)
    query = jnp.dot(normed, w_query, preferred_element_type=jnp.float32)
    keyval = jnp.dot(normed, w_kv, preferred_element_type=jnp.float32)
    cosine, sine_part = rotary_tables(segment, head_dim)
    keys = rotary(keyval[:, :head_dim], cosine, sine_part).astype(jnp.bfloat16)
    values = keyval[:, head_dim:].astype(jnp.bfloat16)
    index = jnp.arange(rows, dtype=jnp.int32)
    allowed = (segment[:, None] == segment[None, :]) & (index[None, :] <= index[:, None])
    stacked = jnp.concatenate(
        [query[:, head * head_dim : (head + 1) * head_dim] for head in range(heads)], 0
    )
    stacked = rotary(
        stacked, jnp.tile(cosine, (heads, 1)), jnp.tile(sine_part, (heads, 1))
    ).astype(jnp.bfloat16)
    scores = lax.dot_general(
        stacked, keys, (((1,), (1,)), ((), ())), preferred_element_type=jnp.float32
    ) / math.sqrt(head_dim)
    expd = jnp.where(jnp.tile(allowed, (heads, 1)), jnp.exp(scores), jnp.zeros_like(scores))
    probs = (expd / jnp.sum(expd, axis=-1, keepdims=True)).astype(jnp.bfloat16)
    mixed = jnp.dot(probs, values, preferred_element_type=jnp.float32).astype(jnp.bfloat16)
    mixed = jnp.concatenate(
        [mixed[head * rows : (head + 1) * rows] for head in range(heads)], -1
    )
    return (values32 + jnp.dot(mixed, w_out, preferred_element_type=jnp.float32)).astype(
        jnp.bfloat16
    )


def relay_forward(value, pieces):
    if pieces < 16:
        return shifted(value, "section", 1)
    first = [(source, source + 1) for source in range(pieces - 1) if source not in (5, 11, 14)]
    first += [(5, 0), (11, 15)]
    second = [(0, 6), (15, 12), (14, 15)]
    where = lax.axis_index("section")
    landed = lax.ppermute(value, "section", first)
    onward = jnp.where((where == 0) | (where == 15), landed, value)
    relayed = lax.ppermute(onward, "section", second)
    late = (where == 6) | (where == 12) | (where == 15)
    landed = jnp.where(where == 0, jnp.zeros_like(landed), landed)
    return jnp.where(late, relayed, landed)


def shards(section_input, stash, cotangent, norm_gain, w_query, w_kv, w_out, doc_ids):
    pieces = lax.axis_size("section")
    mirror = [(source, pieces - 1 - source) for source in range(pieces)]
    fetched = lax.ppermute(stash[0], "section", mirror)
    outward = section_layer(
        section_input[0], norm_gain[0], w_query[0], w_kv[0], w_out[0], doc_ids[0, 0]
    )

    def replay(acts):
        return section_layer(acts, norm_gain[0], w_query[0], w_kv[0], w_out[0], doc_ids[0, 1])

    unused, pullback = jax.vjp(replay, fetched)
    gradient = pullback(cotangent[0])[0]
    forwarded = relay_forward(outward[None], pieces)
    returned = shifted(gradient[None], "section", -1)
    return (forwarded, returned)


def solution(mesh):
    return jax.shard_map(
        shards,
        mesh=mesh,
        in_specs=(
            P(("groups", "section"), None, None),
            P(("groups", "section"), None, None),
            P(("groups", "section"), None, None),
            P("section", None),
            P("section", None, None),
            P("section", None, None),
            P("section", None, None),
            P(("groups", "section"), None, None),
        ),
        out_specs=(P(("groups", "section"), None, None), P(("groups", "section"), None, None)),
        check_vma=False,
    )
```

```python
import math

import jax
import jax.numpy as jnp
from jax import lax
from jax.sharding import PartitionSpec as P


def shifted(value, axis, steps):
    count = lax.axis_size(axis)
    leading, last = (max(0, -steps), min(count, count - steps))
    return lax.ppermute(value, axis, [(source, source + steps) for source in range(leading, last)])


def rotary_tables(segment, head_dim):
    index = jnp.arange(segment.shape[0], dtype=jnp.int32)
    first = jnp.concatenate([jnp.ones((1,), dtype=bool), segment[1:] != segment[:-1]])
    starts = jnp.where(first, index, jnp.zeros_like(index))
    places = (index - lax.cummax(starts, axis=0)).astype(jnp.float32)
    half = head_dim // 2
    freqs = 500000.0 ** (-(jnp.arange(half, dtype=jnp.float32) * 2.0 / head_dim))
    angles = places[:, None] * freqs[None, :]
    cosine = jnp.concatenate([jnp.cos(angles), jnp.cos(angles)], -1)
    sine_part = jnp.concatenate([jnp.sin(angles), jnp.sin(angles)], -1)
    return (cosine, sine_part)


def rotary(block, cosine, sine_part):
    half = block.shape[-1] // 2
    turned = jnp.concatenate([-block[..., half:], block[..., :half]], -1)
    return block * cosine + turned * sine_part


def section_layer(acts, gain, w_query, w_kv, w_out, segment):
    rows = acts.shape[0]
    head_dim = w_kv.shape[1] // 2
    heads = w_query.shape[1] // head_dim
    values32 = acts.astype(jnp.float32)
    scale = lax.rsqrt(jnp.mean(values32 * values32, axis=-1, keepdims=True) + 1e-05)
    normed = (values32 * scale * gain).astype(jnp.bfloat16)
    query = jnp.dot(normed, w_query, preferred_element_type=jnp.float32)
    keyval = jnp.dot(normed, w_kv, preferred_element_type=jnp.float32)
    cosine, sine_part = rotary_tables(segment, head_dim)
    keys = rotary(keyval[:, :head_dim], cosine, sine_part).astype(jnp.bfloat16)
    values = keyval[:, head_dim:].astype(jnp.bfloat16)
    index = jnp.arange(rows, dtype=jnp.int32)
    allowed = (segment[:, None] == segment[None, :]) & (index[None, :] <= index[:, None])
    stacked = jnp.concatenate(
        [query[:, head * head_dim : (head + 1) * head_dim] for head in range(heads)], 0
    )
    stacked = rotary(
        stacked, jnp.tile(cosine, (heads, 1)), jnp.tile(sine_part, (heads, 1))
    ).astype(jnp.bfloat16)
    scores = lax.dot_general(
        stacked, keys, (((1,), (1,)), ((), ())), preferred_element_type=jnp.float32
    ) / math.sqrt(head_dim)
    expd = jnp.where(jnp.tile(allowed, (heads, 1)), jnp.exp(scores), jnp.zeros_like(scores))
    probs = (expd / jnp.sum(expd, axis=-1, keepdims=True)).astype(jnp.bfloat16)
    mixed = jnp.dot(probs, values, preferred_element_type=jnp.float32).astype(jnp.bfloat16)
    mixed = jnp.concatenate(
        [mixed[head * rows : (head + 1) * rows] for head in range(heads)], -1
    )
    return (values32 + jnp.dot(mixed, w_out, preferred_element_type=jnp.float32)).astype(
        jnp.bfloat16
    )


def shards(section_input, stash, cotangent, norm_gain, w_query, w_kv, w_out, doc_ids):
    pieces = lax.axis_size("section")
    mirror = [(source, pieces - 1 - source) for source in range(pieces)]
    fetched = lax.ppermute(stash[0], "section", mirror)
    outward = section_layer(
        section_input[0], norm_gain[0], w_query[0], w_kv[0], w_out[0], doc_ids[0, 0]
    )

    def replay(acts):
        return section_layer(acts, norm_gain[0], w_query[0], w_kv[0], w_out[0], doc_ids[0, 1])

    unused, pullback = jax.vjp(replay, fetched)
    gradient = pullback(cotangent[0])[0]
    forwarded = shifted(outward[None], "section", 1)
    forwarded = jnp.where(lax.axis_index("section") == 0, jnp.zeros_like(forwarded), forwarded)
    returned = shifted(gradient[None], "section", -1)
    return (forwarded, returned)


def solution(mesh):
    return jax.shard_map(
        shards,
        mesh=mesh,
        in_specs=(
            P(("groups", "section"), None, None),
            P(("groups", "section"), None, None),
            P(("groups", "section"), None, None),
            P("section", None),
            P("section", None, None),
            P("section", None, None),
            P("section", None, None),
            P(("groups", "section"), None, None),
        ),
        out_specs=(P(("groups", "section"), None, None), P(("groups", "section"), None, None)),
        check_vma=False,
    )
```

```python
import math

import jax
import jax.numpy as jnp
from jax import lax
from jax.experimental import pallas as pl
from jax.sharding import PartitionSpec as P


def shifted(value, axis, steps):
    count = lax.axis_size(axis)
    leading, last = (max(0, -steps), min(count, count - steps))
    return lax.ppermute(value, axis, [(source, source + steps) for source in range(leading, last)])


def rotary_tables(segment, head_dim):
    index = jnp.arange(segment.shape[0], dtype=jnp.int32)
    first = jnp.concatenate([jnp.ones((1,), dtype=bool), segment[1:] != segment[:-1]])
    starts = jnp.where(first, index, jnp.zeros_like(index))
    places = (index - lax.cummax(starts, axis=0)).astype(jnp.float32)
    half = head_dim // 2
    freqs = 500000.0 ** (-(jnp.arange(half, dtype=jnp.float32) * 2.0 / head_dim))
    angles = places[:, None] * freqs[None, :]
    cosine = jnp.concatenate([jnp.cos(angles), jnp.cos(angles)], -1)
    sine_part = jnp.concatenate([jnp.sin(angles), jnp.sin(angles)], -1)
    return (cosine, sine_part)


def rotary(block, cosine, sine_part):
    half = block.shape[-1] // 2
    turned = jnp.concatenate([-block[..., half:], block[..., :half]], -1)
    return block * cosine + turned * sine_part


def section_layer(acts, gain, w_query, w_kv, w_out, segment):
    rows = acts.shape[0]
    head_dim = w_kv.shape[1] // 2
    heads = w_query.shape[1] // head_dim
    values32 = acts.astype(jnp.float32)
    scale = lax.rsqrt(jnp.mean(values32 * values32, axis=-1, keepdims=True) + 1e-05)
    normed = (values32 * scale * gain).astype(jnp.bfloat16)
    query = jnp.dot(normed, w_query, preferred_element_type=jnp.float32)
    keyval = jnp.dot(normed, w_kv, preferred_element_type=jnp.float32)
    cosine, sine_part = rotary_tables(segment, head_dim)
    keys = rotary(keyval[:, :head_dim], cosine, sine_part).astype(jnp.bfloat16)
    values = keyval[:, head_dim:].astype(jnp.bfloat16)
    index = jnp.arange(rows, dtype=jnp.int32)
    allowed = (segment[:, None] == segment[None, :]) & (index[None, :] <= index[:, None])
    stacked = jnp.concatenate(
        [query[:, head * head_dim : (head + 1) * head_dim] for head in range(heads)], 0
    )
    stacked = rotary(
        stacked, jnp.tile(cosine, (heads, 1)), jnp.tile(sine_part, (heads, 1))
    ).astype(jnp.bfloat16)
    scores = lax.dot_general(
        stacked, keys, (((1,), (1,)), ((), ())), preferred_element_type=jnp.float32
    ) / math.sqrt(head_dim)
    expd = jnp.where(jnp.tile(allowed, (heads, 1)), jnp.exp(scores), jnp.zeros_like(scores))
    probs = (expd / jnp.sum(expd, axis=-1, keepdims=True)).astype(jnp.bfloat16)
    mixed = jnp.dot(probs, values, preferred_element_type=jnp.float32).astype(jnp.bfloat16)
    mixed = jnp.concatenate(
        [mixed[head * rows : (head + 1) * rows] for head in range(heads)], -1
    )
    return (values32 + jnp.dot(mixed, w_out, preferred_element_type=jnp.float32)).astype(
        jnp.bfloat16
    )


def flip(block, sign):
    half = block.shape[-1] // 2
    return jnp.concatenate([sign * block[:, half:], -sign * block[:, :half]], -1)


def attention_gradient_kernel(
    query_ref, keyval_ref, cosine_ref, sine_ref, allowed_ref, upstream_ref, dquery_ref, dkeyval_ref
):
    rows = cosine_ref.shape[0]
    head_dim = cosine_ref.shape[1]
    heads = query_ref.shape[1] // head_dim
    cosine = cosine_ref[...]
    sine_part = sine_ref[...]
    keyval = keyval_ref[...]
    keys = (keyval[:, :head_dim] * cosine + flip(keyval[:, :head_dim], -1.0) * sine_part).astype(
        jnp.bfloat16
    )
    values = keyval[:, head_dim:].astype(jnp.bfloat16)
    query = query_ref[...]
    stacked = jnp.concatenate(
        [query[:, head * head_dim : (head + 1) * head_dim] for head in range(heads)], 0
    )
    cosines = jnp.concatenate([cosine] * heads, 0)
    sines = jnp.concatenate([sine_part] * heads, 0)
    turned = (stacked * cosines + flip(stacked, -1.0) * sines).astype(jnp.bfloat16)
    contract = (((1,), (1,)), ((), ()))
    scores = lax.dot_general(turned, keys, contract, preferred_element_type=jnp.float32)
    scores = scores / math.sqrt(head_dim)
    allowed = jnp.concatenate([allowed_ref[...]] * heads, 0) > 0
    raised = jnp.exp(scores)
    expd = jnp.where(allowed, raised, 0.0)
    total = jnp.sum(expd, axis=-1, keepdims=True)
    probs = (expd / total).astype(jnp.bfloat16)
    upstream = upstream_ref[...]
    dmixed = jnp.concatenate(
        [upstream[:, head * head_dim : (head + 1) * head_dim] for head in range(heads)], 0
    )
    dprobs = lax.dot_general(dmixed, values, contract, preferred_element_type=jnp.float32)
    dprobs = dprobs.astype(jnp.bfloat16).astype(jnp.float32)
    dvalues = lax.dot_general(
        probs, dmixed, (((0,), (0,)), ((), ())), preferred_element_type=jnp.float32
    ).astype(jnp.bfloat16)
    dtotal = -jnp.sum(dprobs * expd / (total * total), axis=-1, keepdims=True)
    dexpd = dprobs / total + dtotal
    dscores = (jnp.where(allowed, dexpd, 0.0) * raised / math.sqrt(head_dim)).astype(jnp.bfloat16)
    dturned = jnp.dot(dscores, keys, preferred_element_type=jnp.float32)
    dturned = dturned.astype(jnp.bfloat16).astype(jnp.float32)
    dkeys = lax.dot_general(
        dscores, turned, (((0,), (0,)), ((), ())), preferred_element_type=jnp.float32
    )
    dkeys = dkeys.astype(jnp.bfloat16).astype(jnp.float32)
    dstacked = dturned * cosines + flip(dturned * sines, 1.0)
    dquery_ref[...] = jnp.concatenate(
        [dstacked[head * rows : (head + 1) * rows] for head in range(heads)], 1
    )
    dkeyval_ref[...] = jnp.concatenate(
        [dkeys * cosine + flip(dkeys * sine_part, 1.0), dvalues.astype(jnp.float32)], 1
    )


def attention_gradient(query, keyval, cosine, sine_part, allowed, dmixed):
    return pl.pallas_call(
        attention_gradient_kernel,
        out_shape=(
            jax.ShapeDtypeStruct(query.shape, jnp.float32),
            jax.ShapeDtypeStruct(keyval.shape, jnp.float32),
        ),
    )(query, keyval, cosine, sine_part, allowed, dmixed)


def input_gradient(acts, cotangent, gain, w_query, w_kv, w_out, segment):
    rows = acts.shape[0]
    head_dim = w_kv.shape[1] // 2

    def project(values32):
        scale = lax.rsqrt(jnp.mean(values32 * values32, axis=-1, keepdims=True) + 1e-05)
        normed = (values32 * scale * gain).astype(jnp.bfloat16)
        query = jnp.dot(normed, w_query, preferred_element_type=jnp.float32)
        keyval = jnp.dot(normed, w_kv, preferred_element_type=jnp.float32)
        return (query, keyval)

    cosine, sine_part = rotary_tables(segment, head_dim)
    index = jnp.arange(rows, dtype=jnp.int32)
    allowed = (segment[:, None] == segment[None, :]) & (index[None, :] <= index[:, None])
    dmixed = lax.dot_general(
        cotangent, w_out, (((1,), (1,)), ((), ())), preferred_element_type=jnp.float32
    ).astype(jnp.bfloat16)
    values32 = acts.astype(jnp.float32)
    (query, keyval), pullback = jax.vjp(project, values32)
    dquery, dkeyval = attention_gradient(
        query, keyval, cosine, sine_part, allowed.astype(jnp.float32), dmixed
    )
    dvalues32 = pullback((dquery, dkeyval))[0]
    return (cotangent.astype(jnp.float32) + dvalues32).astype(jnp.bfloat16)


def shards(section_input, stash, cotangent, norm_gain, w_query, w_kv, w_out, doc_ids):
    pieces = lax.axis_size("section")
    mirror = [(source, pieces - 1 - source) for source in range(pieces)]
    fetched = lax.ppermute(stash[0], "section", mirror)
    outward = section_layer(
        section_input[0], norm_gain[0], w_query[0], w_kv[0], w_out[0], doc_ids[0, 0]
    )
    gradient = input_gradient(
        fetched, cotangent[0], norm_gain[0], w_query[0], w_kv[0], w_out[0], doc_ids[0, 1]
    )
    forwarded = shifted(outward[None], "section", 1)
    returned = shifted(gradient[None], "section", -1)
    return (forwarded, returned)


def solution(mesh):
    return jax.shard_map(
        shards,
        mesh=mesh,
        in_specs=(
            P(("groups", "section"), None, None),
            P(("groups", "section"), None, None),
            P(("groups", "section"), None, None),
            P("section", None),
            P("section", None, None),
            P("section", None, None),
            P("section", None, None),
            P(("groups", "section"), None, None),
        ),
        out_specs=(P(("groups", "section"), None, None), P(("groups", "section"), None, None)),
        check_vma=False,
    )
```

```python
import math

import jax
import jax.numpy as jnp
from jax import lax
from jax.experimental import pallas as pl
from jax.sharding import PartitionSpec as P


def shifted(value, axis, steps):
    count = lax.axis_size(axis)
    leading, last = (max(0, -steps), min(count, count - steps))
    return lax.ppermute(value, axis, [(source, source + steps) for source in range(leading, last)])


def rotary_tables(segment, head_dim):
    index = jnp.arange(segment.shape[0], dtype=jnp.int32)
    first = jnp.concatenate([jnp.ones((1,), dtype=bool), segment[1:] != segment[:-1]])
    starts = jnp.where(first, index, jnp.zeros_like(index))
    places = (index - lax.cummax(starts, axis=0)).astype(jnp.float32)
    half = head_dim // 2
    freqs = 500000.0 ** (-(jnp.arange(half, dtype=jnp.float32) * 2.0 / head_dim))
    angles = places[:, None] * freqs[None, :]
    cosine = jnp.concatenate([jnp.cos(angles), jnp.cos(angles)], -1)
    sine_part = jnp.concatenate([jnp.sin(angles), jnp.sin(angles)], -1)
    return (cosine, sine_part)


def rotary(block, cosine, sine_part):
    half = block.shape[-1] // 2
    turned = jnp.concatenate([-block[..., half:], block[..., :half]], -1)
    return block * cosine + turned * sine_part


def section_layer(acts, gain, w_query, w_kv, w_out, segment):
    rows = acts.shape[0]
    head_dim = w_kv.shape[1] // 2
    heads = w_query.shape[1] // head_dim
    values32 = acts.astype(jnp.float32)
    scale = lax.rsqrt(jnp.mean(values32 * values32, axis=-1, keepdims=True) + 1e-05)
    normed = (values32 * scale * gain).astype(jnp.bfloat16)
    query = jnp.dot(normed, w_query, preferred_element_type=jnp.float32)
    keyval = jnp.dot(normed, w_kv, preferred_element_type=jnp.float32)
    cosine, sine_part = rotary_tables(segment, head_dim)
    keys = rotary(keyval[:, :head_dim], cosine, sine_part).astype(jnp.bfloat16)
    values = keyval[:, head_dim:].astype(jnp.bfloat16)
    index = jnp.arange(rows, dtype=jnp.int32)
    allowed = (segment[:, None] == segment[None, :]) & (index[None, :] <= index[:, None])
    stacked = jnp.concatenate(
        [query[:, head * head_dim : (head + 1) * head_dim] for head in range(heads)], 0
    )
    stacked = rotary(
        stacked, jnp.tile(cosine, (heads, 1)), jnp.tile(sine_part, (heads, 1))
    ).astype(jnp.bfloat16)
    scores = lax.dot_general(
        stacked, keys, (((1,), (1,)), ((), ())), preferred_element_type=jnp.float32
    ) / math.sqrt(head_dim)
    expd = jnp.where(jnp.tile(allowed, (heads, 1)), jnp.exp(scores), jnp.zeros_like(scores))
    probs = (expd / jnp.sum(expd, axis=-1, keepdims=True)).astype(jnp.bfloat16)
    mixed = jnp.dot(probs, values, preferred_element_type=jnp.float32).astype(jnp.bfloat16)
    mixed = jnp.concatenate(
        [mixed[head * rows : (head + 1) * rows] for head in range(heads)], -1
    )
    return (values32 + jnp.dot(mixed, w_out, preferred_element_type=jnp.float32)).astype(
        jnp.bfloat16
    )


def flip(block, sign):
    half = block.shape[-1] // 2
    return jnp.concatenate([sign * block[:, half:], -sign * block[:, :half]], -1)


def attention_gradient_body(query, keyval, cosine, sine_part, allowed, upstream):
    rows = cosine.shape[0]
    head_dim = cosine.shape[1]
    heads = query.shape[1] // head_dim
    keys = (keyval[:, :head_dim] * cosine + flip(keyval[:, :head_dim], -1.0) * sine_part).astype(
        jnp.bfloat16
    )
    values = keyval[:, head_dim:].astype(jnp.bfloat16)
    stacked = jnp.concatenate(
        [query[:, head * head_dim : (head + 1) * head_dim] for head in range(heads)], 0
    )
    cosines = jnp.concatenate([cosine] * heads, 0)
    sines = jnp.concatenate([sine_part] * heads, 0)
    turned = (stacked * cosines + flip(stacked, -1.0) * sines).astype(jnp.bfloat16)
    contract = (((1,), (1,)), ((), ()))
    scores = lax.dot_general(turned, keys, contract, preferred_element_type=jnp.float32)
    scores = scores / math.sqrt(head_dim)
    allowed = jnp.concatenate([allowed] * heads, 0) > 0
    raised = jnp.exp(scores)
    expd = jnp.where(allowed, raised, 0.0)
    total = jnp.sum(expd, axis=-1, keepdims=True)
    probs = (expd / total).astype(jnp.bfloat16)
    dmixed = jnp.concatenate(
        [upstream[:, head * head_dim : (head + 1) * head_dim] for head in range(heads)], 0
    )
    dprobs = lax.dot_general(dmixed, values, contract, preferred_element_type=jnp.float32)
    dprobs = dprobs.astype(jnp.bfloat16).astype(jnp.float32)
    dvalues = lax.dot_general(
        probs, dmixed, (((0,), (0,)), ((), ())), preferred_element_type=jnp.float32
    ).astype(jnp.bfloat16)
    dtotal = -jnp.sum(dprobs * expd / (total * total), axis=-1, keepdims=True)
    dexpd = dprobs / total + dtotal
    dscores = (jnp.where(allowed, dexpd, 0.0) * raised / math.sqrt(head_dim)).astype(jnp.bfloat16)
    dturned = jnp.dot(dscores, keys, preferred_element_type=jnp.float32)
    dturned = dturned.astype(jnp.bfloat16).astype(jnp.float32)
    dkeys = lax.dot_general(
        dscores, turned, (((0,), (0,)), ((), ())), preferred_element_type=jnp.float32
    )
    dkeys = dkeys.astype(jnp.bfloat16).astype(jnp.float32)
    dstacked = dturned * cosines + flip(dturned * sines, 1.0)
    dquery = jnp.concatenate(
        [dstacked[head * rows : (head + 1) * rows] for head in range(heads)], 1
    )
    dkeyval = jnp.concatenate(
        [dkeys * cosine + flip(dkeys * sine_part, 1.0), dvalues.astype(jnp.float32)], 1
    )
    return (dquery, dkeyval)


def input_gradient_kernel(
    acts_ref, cotangent_ref, gain_ref, wq_ref, wkv_ref, cosine_ref, sine_ref, allowed_ref,
    upstream_ref, out_ref,
):
    values32 = acts_ref[...].astype(jnp.float32)
    gain = gain_ref[...]
    width = values32.shape[1]
    scale = lax.rsqrt(jnp.sum(values32 * values32, axis=-1, keepdims=True) / width + 1e-05)
    normed = (values32 * scale * gain).astype(jnp.bfloat16)
    w_query = wq_ref[...]
    w_kv = wkv_ref[...]
    query = jnp.dot(normed, w_query, preferred_element_type=jnp.float32)
    keyval = jnp.dot(normed, w_kv, preferred_element_type=jnp.float32)
    dquery, dkeyval = attention_gradient_body(
        query, keyval, cosine_ref[...], sine_ref[...], allowed_ref[...], upstream_ref[...]
    )
    contract = (((1,), (1,)), ((), ()))
    from_query = lax.dot_general(
        dquery.astype(jnp.bfloat16), w_query, contract, preferred_element_type=jnp.float32
    ).astype(jnp.bfloat16)
    from_keyval = lax.dot_general(
        dkeyval.astype(jnp.bfloat16), w_kv, contract, preferred_element_type=jnp.float32
    ).astype(jnp.bfloat16)
    dnormed = (from_query.astype(jnp.float32) + from_keyval.astype(jnp.float32)).astype(
        jnp.bfloat16
    ).astype(jnp.float32)
    weighted = dnormed * gain
    spread = jnp.sum(weighted * values32, axis=-1, keepdims=True) * (scale * scale * scale) / width
    dvalues32 = weighted * scale - values32 * spread
    out_ref[...] = (cotangent_ref[...].astype(jnp.float32) + dvalues32).astype(out_ref.dtype)


def input_gradient(acts, cotangent, gain, w_query, w_kv, w_out, segment):
    rows = acts.shape[0]
    head_dim = w_kv.shape[1] // 2
    cosine, sine_part = rotary_tables(segment, head_dim)
    index = jnp.arange(rows, dtype=jnp.int32)
    allowed = (segment[:, None] == segment[None, :]) & (index[None, :] <= index[:, None])
    dmixed = lax.dot_general(
        cotangent, w_out, (((1,), (1,)), ((), ())), preferred_element_type=jnp.float32
    ).astype(jnp.bfloat16)
    return pl.pallas_call(
        input_gradient_kernel, out_shape=jax.ShapeDtypeStruct(acts.shape, acts.dtype)
    )(
        acts, cotangent, gain.reshape(1, -1), w_query, w_kv, cosine, sine_part,
        allowed.astype(jnp.float32), dmixed,
    )


def shards(section_input, stash, cotangent, norm_gain, w_query, w_kv, w_out, doc_ids):
    pieces = lax.axis_size("section")
    mirror = [(source, pieces - 1 - source) for source in range(pieces)]
    fetched = lax.ppermute(stash[0], "section", mirror)
    outward = section_layer(
        section_input[0], norm_gain[0], w_query[0], w_kv[0], w_out[0], doc_ids[0, 0]
    )
    gradient = input_gradient(
        fetched, cotangent[0], norm_gain[0], w_query[0], w_kv[0], w_out[0], doc_ids[0, 1]
    )
    forwarded = shifted(outward[None], "section", 1)
    returned = shifted(gradient[None], "section", -1)
    return (forwarded, returned)


def solution(mesh):
    return jax.shard_map(
        shards,
        mesh=mesh,
        in_specs=(
            P(("groups", "section"), None, None),
            P(("groups", "section"), None, None),
            P(("groups", "section"), None, None),
            P("section", None),
            P("section", None, None),
            P("section", None, None),
            P("section", None, None),
            P(("groups", "section"), None, None),
        ),
        out_specs=(P(("groups", "section"), None, None), P(("groups", "section"), None, None)),
        check_vma=False,
    )
```

```python
import math

import jax
import jax.numpy as jnp
from jax import lax
from jax.experimental import pallas as pl
from jax.sharding import PartitionSpec as P


def shifted(value, axis, steps):
    count = lax.axis_size(axis)
    leading, last = (max(0, -steps), min(count, count - steps))
    return lax.ppermute(value, axis, [(source, source + steps) for source in range(leading, last)])


def rotary_tables(segment, head_dim):
    index = jnp.arange(segment.shape[0], dtype=jnp.int32)
    first = jnp.concatenate([jnp.ones((1,), dtype=bool), segment[1:] != segment[:-1]])
    starts = jnp.where(first, index, jnp.zeros_like(index))
    places = (index - lax.cummax(starts, axis=0)).astype(jnp.float32)
    half = head_dim // 2
    freqs = 500000.0 ** (-(jnp.arange(half, dtype=jnp.float32) * 2.0 / head_dim))
    angles = places[:, None] * freqs[None, :]
    cosine = jnp.concatenate([jnp.cos(angles), jnp.cos(angles)], -1)
    sine_part = jnp.concatenate([jnp.sin(angles), jnp.sin(angles)], -1)
    return (cosine, sine_part)


def rotary(block, cosine, sine_part):
    half = block.shape[-1] // 2
    turned = jnp.concatenate([-block[..., half:], block[..., :half]], -1)
    return block * cosine + turned * sine_part


def section_layer(acts, gain, w_query, w_kv, w_out, segment):
    rows = acts.shape[0]
    head_dim = w_kv.shape[1] // 2
    heads = w_query.shape[1] // head_dim
    values32 = acts.astype(jnp.float32)
    scale = lax.rsqrt(jnp.mean(values32 * values32, axis=-1, keepdims=True) + 1e-05)
    normed = (values32 * scale * gain).astype(jnp.bfloat16)
    query = jnp.dot(normed, w_query, preferred_element_type=jnp.float32)
    keyval = jnp.dot(normed, w_kv, preferred_element_type=jnp.float32)
    cosine, sine_part = rotary_tables(segment, head_dim)
    keys = rotary(keyval[:, :head_dim], cosine, sine_part).astype(jnp.bfloat16)
    values = keyval[:, head_dim:].astype(jnp.bfloat16)
    index = jnp.arange(rows, dtype=jnp.int32)
    allowed = (segment[:, None] == segment[None, :]) & (index[None, :] <= index[:, None])
    stacked = jnp.concatenate(
        [query[:, head * head_dim : (head + 1) * head_dim] for head in range(heads)], 0
    )
    stacked = rotary(
        stacked, jnp.tile(cosine, (heads, 1)), jnp.tile(sine_part, (heads, 1))
    ).astype(jnp.bfloat16)
    scores = lax.dot_general(
        stacked, keys, (((1,), (1,)), ((), ())), preferred_element_type=jnp.float32
    ) / math.sqrt(head_dim)
    expd = jnp.where(jnp.tile(allowed, (heads, 1)), jnp.exp(scores), jnp.zeros_like(scores))
    probs = (expd / jnp.sum(expd, axis=-1, keepdims=True)).astype(jnp.bfloat16)
    mixed = jnp.dot(probs, values, preferred_element_type=jnp.float32).astype(jnp.bfloat16)
    mixed = jnp.concatenate(
        [mixed[head * rows : (head + 1) * rows] for head in range(heads)], -1
    )
    return (values32 + jnp.dot(mixed, w_out, preferred_element_type=jnp.float32)).astype(
        jnp.bfloat16
    )


def flip(block, sign):
    half = block.shape[-1] // 2
    return jnp.concatenate([sign * block[:, half:], -sign * block[:, :half]], -1)


def attention_gradient_body(query, keyval, cosine, sine_part, allowed, upstream):
    rows = cosine.shape[0]
    head_dim = cosine.shape[1]
    heads = query.shape[1] // head_dim
    keys = (keyval[:, :head_dim] * cosine + flip(keyval[:, :head_dim], -1.0) * sine_part).astype(
        jnp.bfloat16
    )
    values = keyval[:, head_dim:].astype(jnp.bfloat16)
    stacked = jnp.concatenate(
        [query[:, head * head_dim : (head + 1) * head_dim] for head in range(heads)], 0
    )
    cosines = jnp.concatenate([cosine] * heads, 0)
    sines = jnp.concatenate([sine_part] * heads, 0)
    turned = (stacked * cosines + flip(stacked, -1.0) * sines).astype(jnp.bfloat16)
    contract = (((1,), (1,)), ((), ()))
    scores = lax.dot_general(turned, keys, contract, preferred_element_type=jnp.float32)
    scores = scores / math.sqrt(head_dim)
    allowed = jnp.concatenate([allowed] * heads, 0) > 0
    raised = jnp.exp(scores)
    expd = jnp.where(allowed, raised, 0.0)
    total = jnp.sum(expd, axis=-1, keepdims=True)
    probs = (expd / total).astype(jnp.bfloat16)
    dmixed = jnp.concatenate(
        [upstream[:, head * head_dim : (head + 1) * head_dim] for head in range(heads)], 0
    )
    dprobs = lax.dot_general(dmixed, values, contract, preferred_element_type=jnp.float32)
    dprobs = dprobs.astype(jnp.bfloat16).astype(jnp.float32)
    dvalues = lax.dot_general(
        probs, dmixed, (((0,), (0,)), ((), ())), preferred_element_type=jnp.float32
    ).astype(jnp.bfloat16)
    dtotal = -jnp.sum(dprobs * expd / (total * total), axis=-1, keepdims=True)
    dexpd = dprobs / total + dtotal
    dscores = (jnp.where(allowed, dexpd, 0.0) * raised / math.sqrt(head_dim)).astype(jnp.bfloat16)
    dturned = jnp.dot(dscores, keys, preferred_element_type=jnp.float32)
    dturned = dturned.astype(jnp.bfloat16).astype(jnp.float32)
    dkeys = lax.dot_general(
        dscores, turned, (((0,), (0,)), ((), ())), preferred_element_type=jnp.float32
    )
    dkeys = dkeys.astype(jnp.bfloat16).astype(jnp.float32)
    dstacked = dturned * cosines + flip(dturned * sines, 1.0)
    dquery = jnp.concatenate(
        [dstacked[head * rows : (head + 1) * rows] for head in range(heads)], 1
    )
    dkeyval = jnp.concatenate(
        [dkeys * cosine + flip(dkeys * sine_part, 1.0), dvalues.astype(jnp.float32)], 1
    )
    return (dquery, dkeyval)


def input_gradient_kernel(
    acts_ref, cotangent_ref, gain_ref, weight_ref, cosine_ref, sine_ref, allowed_ref,
    upstream_ref, out_ref,
):
    values32 = acts_ref[...].astype(jnp.float32)
    gain = gain_ref[...]
    width = values32.shape[1]
    split = upstream_ref.shape[1]
    scale = lax.rsqrt(jnp.sum(values32 * values32, axis=-1, keepdims=True) / width + 1e-05)
    weight = weight_ref[...]
    projected = jnp.dot(
        (values32 * (scale * gain)).astype(jnp.bfloat16), weight, preferred_element_type=jnp.float32
    )
    dquery, dkeyval = attention_gradient_body(
        projected[:, :split], projected[:, split:], cosine_ref[...], sine_ref[...],
        allowed_ref[...], upstream_ref[...],
    )
    both = jnp.concatenate([dquery, dkeyval], 1).astype(jnp.bfloat16)
    dnormed = lax.dot_general(
        both, weight, (((1,), (1,)), ((), ())), preferred_element_type=jnp.float32
    ).astype(jnp.bfloat16).astype(jnp.float32)
    weighted = dnormed * gain
    spread = jnp.sum(weighted * values32, axis=-1, keepdims=True) * (scale * scale * scale) / width
    out_ref[...] = (
        cotangent_ref[...].astype(jnp.float32) + weighted * scale - values32 * spread
    ).astype(out_ref.dtype)


def input_gradient(acts, cotangent, gain, w_query, w_kv, w_out, segment):
    rows = acts.shape[0]
    head_dim = w_kv.shape[1] // 2
    cosine, sine_part = rotary_tables(segment, head_dim)
    index = jnp.arange(rows, dtype=jnp.int32)
    allowed = (segment[:, None] == segment[None, :]) & (index[None, :] <= index[:, None])
    dmixed = lax.dot_general(
        cotangent, w_out, (((1,), (1,)), ((), ())), preferred_element_type=jnp.float32
    ).astype(jnp.bfloat16)
    return pl.pallas_call(
        input_gradient_kernel, out_shape=jax.ShapeDtypeStruct(acts.shape, acts.dtype)
    )(
        acts, cotangent, gain.reshape(1, -1), jnp.concatenate([w_query, w_kv], 1), cosine, sine_part,
        allowed.astype(jnp.float32), dmixed,
    )


def shards(section_input, stash, cotangent, norm_gain, w_query, w_kv, w_out, doc_ids):
    pieces = lax.axis_size("section")
    mirror = [(source, pieces - 1 - source) for source in range(pieces)]
    fetched = lax.ppermute(stash[0], "section", mirror)
    outward = section_layer(
        section_input[0], norm_gain[0], w_query[0], w_kv[0], w_out[0], doc_ids[0, 0]
    )
    gradient = input_gradient(
        fetched, cotangent[0], norm_gain[0], w_query[0], w_kv[0], w_out[0], doc_ids[0, 1]
    )
    forwarded = shifted(outward[None], "section", 1)
    returned = shifted(gradient[None], "section", -1)
    return (forwarded, returned)


def solution(mesh):
    return jax.shard_map(
        shards,
        mesh=mesh,
        in_specs=(
            P(("groups", "section"), None, None),
            P(("groups", "section"), None, None),
            P(("groups", "section"), None, None),
            P("section", None),
            P("section", None, None),
            P("section", None, None),
            P("section", None, None),
            P(("groups", "section"), None, None),
        ),
        out_specs=(P(("groups", "section"), None, None), P(("groups", "section"), None, None)),
        check_vma=False,
    )
```

```python
import math

import jax
import jax.numpy as jnp
from jax import lax
from jax.sharding import PartitionSpec as P


def shifted(value, axis, steps):
    count = lax.axis_size(axis)
    leading, last = (max(0, -steps), min(count, count - steps))
    return lax.ppermute(value, axis, [(source, source + steps) for source in range(leading, last)])


def rotary_tables(segment, head_dim):
    index = jnp.arange(segment.shape[0], dtype=jnp.int32)
    first = jnp.concatenate([jnp.ones((1,), dtype=bool), segment[1:] != segment[:-1]])
    starts = jnp.where(first, index, jnp.zeros_like(index))
    places = (index - lax.cummax(starts, axis=0)).astype(jnp.float32)
    half = head_dim // 2
    freqs = 500000.0 ** (-(jnp.arange(half, dtype=jnp.float32) * 2.0 / head_dim))
    angles = places[:, None] * freqs[None, :]
    cosine = jnp.concatenate([jnp.cos(angles), jnp.cos(angles)], -1)
    sine_part = jnp.concatenate([jnp.sin(angles), jnp.sin(angles)], -1)
    return (cosine, sine_part)


def rotary(block, cosine, sine_part):
    half = block.shape[-1] // 2
    turned = jnp.concatenate([-block[..., half:], block[..., :half]], -1)
    return block * cosine + turned * sine_part


def section_layer(acts, gain, w_query, w_kv, w_out, segment):
    rows = acts.shape[0]
    head_dim = w_kv.shape[1] // 2
    heads = w_query.shape[1] // head_dim
    values32 = acts.astype(jnp.float32)
    scale = lax.rsqrt(jnp.mean(values32 * values32, axis=-1, keepdims=True) + 1e-05)
    normed = (values32 * scale * gain).astype(jnp.bfloat16)
    query = jnp.dot(normed, w_query, preferred_element_type=jnp.float32)
    keyval = jnp.dot(normed, w_kv, preferred_element_type=jnp.float32)
    cosine, sine_part = rotary_tables(segment, head_dim)
    keys = rotary(keyval[:, :head_dim], cosine, sine_part).astype(jnp.bfloat16)
    values = keyval[:, head_dim:].astype(jnp.bfloat16)
    index = jnp.arange(rows, dtype=jnp.int32)
    allowed = (segment[:, None] == segment[None, :]) & (index[None, :] <= index[:, None])
    stacked = jnp.concatenate(
        [query[:, head * head_dim : (head + 1) * head_dim] for head in range(heads)], 0
    )
    stacked = rotary(
        stacked, jnp.tile(cosine, (heads, 1)), jnp.tile(sine_part, (heads, 1))
    ).astype(jnp.bfloat16)
    scores = lax.dot_general(
        stacked, keys, (((1,), (1,)), ((), ())), preferred_element_type=jnp.float32
    ) / math.sqrt(head_dim)
    expd = jnp.where(jnp.tile(allowed, (heads, 1)), jnp.exp(scores), jnp.zeros_like(scores))
    probs = (expd / jnp.sum(expd, axis=-1, keepdims=True)).astype(jnp.bfloat16)
    mixed = jnp.dot(probs, values, preferred_element_type=jnp.float32).astype(jnp.bfloat16)
    mixed = jnp.concatenate(
        [mixed[head * rows : (head + 1) * rows] for head in range(heads)], -1
    )
    return (values32 + jnp.dot(mixed, w_out, preferred_element_type=jnp.float32)).astype(
        jnp.bfloat16
    )


def attention_part(query, keyval, segment, head_dim):
    rows = query.shape[0]
    heads = query.shape[1] // head_dim
    cosine, sine_part = rotary_tables(segment, head_dim)
    keys = rotary(keyval[:, :head_dim], cosine, sine_part).astype(jnp.bfloat16)
    values = keyval[:, head_dim:].astype(jnp.bfloat16)
    index = jnp.arange(rows, dtype=jnp.int32)
    allowed = (segment[:, None] == segment[None, :]) & (index[None, :] <= index[:, None])
    stacked = jnp.concatenate(
        [query[:, head * head_dim : (head + 1) * head_dim] for head in range(heads)], 0
    )
    stacked = rotary(
        stacked, jnp.tile(cosine, (heads, 1)), jnp.tile(sine_part, (heads, 1))
    ).astype(jnp.bfloat16)
    scores = lax.dot_general(
        stacked, keys, (((1,), (1,)), ((), ())), preferred_element_type=jnp.float32
    ) / math.sqrt(head_dim)
    expd = jnp.where(jnp.tile(allowed, (heads, 1)), jnp.exp(scores), jnp.zeros_like(scores))
    probs = (expd / jnp.sum(expd, axis=-1, keepdims=True)).astype(jnp.bfloat16)
    mixed = jnp.dot(probs, values, preferred_element_type=jnp.float32).astype(jnp.bfloat16)
    return jnp.concatenate([mixed[head * rows : (head + 1) * rows] for head in range(heads)], -1)


def gradient_halves(acts, cotangent, gain, w_query, w_kv, w_out, segment):
    rows = acts.shape[0]
    width = acts.shape[1]
    head_dim = w_kv.shape[1] // 2
    values32 = acts.astype(jnp.float32)
    scale = lax.rsqrt(jnp.mean(values32 * values32, axis=-1, keepdims=True) + 1e-05)
    normed = (values32 * scale * gain).astype(jnp.bfloat16)
    query = jnp.dot(normed, w_query, preferred_element_type=jnp.float32)
    keyval = jnp.dot(normed, w_kv, preferred_element_type=jnp.float32)
    dmixed = lax.dot_general(
        cotangent, w_out, (((1,), (1,)), ((), ())), preferred_element_type=jnp.float32
    ).astype(jnp.bfloat16)
    unused, pullback = jax.vjp(
        lambda q, kv: attention_part(q, kv, segment, head_dim), query, keyval
    )
    dquery, dkeyval = pullback(dmixed)
    contract = (((1,), (1,)), ((), ()))
    halves = []
    for low in (0, rows // 2):
        part = slice(low, low + rows // 2)
        from_query = lax.dot_general(
            dquery[part], w_query, contract, preferred_element_type=jnp.bfloat16
        )
        from_keyval = lax.dot_general(
            dkeyval[part], w_kv, contract, preferred_element_type=jnp.bfloat16
        )
        weighted = (from_query + from_keyval).astype(jnp.float32) * gain
        own = values32[part]
        spread = jnp.sum(weighted * own, axis=-1, keepdims=True) * scale[part] ** 3 / width
        grad = weighted * scale[part] - own * spread
        halves.append((cotangent[part].astype(jnp.float32) + grad).astype(jnp.bfloat16))
    return halves


def shards(section_input, stash, cotangent, norm_gain, w_query, w_kv, w_out, doc_ids):
    pieces = lax.axis_size("section")
    mirror = [(source, pieces - 1 - source) for source in range(pieces)]
    fetched = lax.ppermute(stash[0], "section", mirror)
    outward = section_layer(
        section_input[0], norm_gain[0], w_query[0], w_kv[0], w_out[0], doc_ids[0, 0]
    )
    halves = gradient_halves(
        fetched, cotangent[0], norm_gain[0], w_query[0], w_kv[0], w_out[0], doc_ids[0, 1]
    )
    forwarded = shifted(outward[None], "section", 1)
    returned = jnp.concatenate([shifted(half[None], "section", -1) for half in halves], 1)
    return (forwarded, returned)


def solution(mesh):
    return jax.shard_map(
        shards,
        mesh=mesh,
        in_specs=(
            P(("groups", "section"), None, None),
            P(("groups", "section"), None, None),
            P(("groups", "section"), None, None),
            P("section", None),
            P("section", None, None),
            P("section", None, None),
            P("section", None, None),
            P(("groups", "section"), None, None),
        ),
        out_specs=(P(("groups", "section"), None, None), P(("groups", "section"), None, None)),
        check_vma=False,
    )
```

```python
import math

import jax
import jax.numpy as jnp
from jax import lax
from jax.sharding import PartitionSpec as P


def shifted(value, axis, steps):
    count = lax.axis_size(axis)
    leading, last = (max(0, -steps), min(count, count - steps))
    return lax.ppermute(value, axis, [(source, source + steps) for source in range(leading, last)])


def rotary_tables(segment, head_dim):
    index = jnp.arange(segment.shape[0], dtype=jnp.int32)
    first = jnp.concatenate([jnp.ones((1,), dtype=bool), segment[1:] != segment[:-1]])
    starts = jnp.where(first, index, jnp.zeros_like(index))
    places = (index - lax.cummax(starts, axis=0)).astype(jnp.float32)
    half = head_dim // 2
    freqs = 500000.0 ** (-(jnp.arange(half, dtype=jnp.float32) * 2.0 / head_dim))
    angles = places[:, None] * freqs[None, :]
    cosine = jnp.concatenate([jnp.cos(angles), jnp.cos(angles)], -1)
    sine_part = jnp.concatenate([jnp.sin(angles), jnp.sin(angles)], -1)
    return (cosine, sine_part)


def rotary(block, cosine, sine_part):
    half = block.shape[-1] // 2
    turned = jnp.concatenate([-block[..., half:], block[..., :half]], -1)
    return block * cosine + turned * sine_part


def section_layer(acts, gain, w_query, w_kv, w_out, segment):
    rows = acts.shape[0]
    head_dim = w_kv.shape[1] // 2
    heads = w_query.shape[1] // head_dim
    values32 = acts.astype(jnp.float32)
    scale = lax.rsqrt(jnp.mean(values32 * values32, axis=-1, keepdims=True) + 1e-05)
    normed = (values32 * scale * gain).astype(jnp.bfloat16)
    query = jnp.dot(normed, w_query, preferred_element_type=jnp.float32)
    keyval = jnp.dot(normed, w_kv, preferred_element_type=jnp.float32)
    cosine, sine_part = rotary_tables(segment, head_dim)
    keys = rotary(keyval[:, :head_dim], cosine, sine_part).astype(jnp.bfloat16)
    values = keyval[:, head_dim:].astype(jnp.bfloat16)
    index = jnp.arange(rows, dtype=jnp.int32)
    allowed = (segment[:, None] == segment[None, :]) & (index[None, :] <= index[:, None])
    stacked = jnp.concatenate(
        [query[:, head * head_dim : (head + 1) * head_dim] for head in range(heads)], 0
    )
    stacked = rotary(
        stacked, jnp.tile(cosine, (heads, 1)), jnp.tile(sine_part, (heads, 1))
    ).astype(jnp.bfloat16)
    scores = lax.dot_general(
        stacked, keys, (((1,), (1,)), ((), ())), preferred_element_type=jnp.float32
    ) / math.sqrt(head_dim)
    expd = jnp.where(jnp.tile(allowed, (heads, 1)), jnp.exp(scores), jnp.zeros_like(scores))
    probs = (expd / jnp.sum(expd, axis=-1, keepdims=True)).astype(jnp.bfloat16)
    mixed = jnp.dot(probs, values, preferred_element_type=jnp.float32).astype(jnp.bfloat16)
    mixed = jnp.concatenate(
        [mixed[head * rows : (head + 1) * rows] for head in range(heads)], -1
    )
    return (values32 + jnp.dot(mixed, w_out, preferred_element_type=jnp.float32)).astype(
        jnp.bfloat16
    )


def relay_forward(value, pieces):
    if pieces < 16:
        return shifted(value, "section", 1)
    first = [(source, source + 1) for source in range(pieces - 1) if source not in (5, 11, 14)]
    first += [(11, 15)]
    second = [(5, 6), (15, 12), (14, 15)]
    where = lax.axis_index("section")
    landed = lax.ppermute(value, "section", first)
    onward = jnp.where(where == 15, landed, value)
    late = lax.ppermute(onward, "section", second)
    tail = (where == 6) | (where == 12) | (where == 15)
    return jnp.where(tail, late, landed)


def shards(section_input, stash, cotangent, norm_gain, w_query, w_kv, w_out, doc_ids):
    pieces = lax.axis_size("section")
    mirror = [(source, pieces - 1 - source) for source in range(pieces)]
    fetched = lax.ppermute(stash[0], "section", mirror)
    outward = section_layer(
        section_input[0], norm_gain[0], w_query[0], w_kv[0], w_out[0], doc_ids[0, 0]
    )

    def replay(acts):
        return section_layer(acts, norm_gain[0], w_query[0], w_kv[0], w_out[0], doc_ids[0, 1])

    unused, pullback = jax.vjp(replay, fetched)
    gradient = pullback(cotangent[0])[0]
    forwarded = relay_forward(outward[None], pieces)
    returned = shifted(gradient[None], "section", -1)
    return (forwarded, returned)


def solution(mesh):
    return jax.shard_map(
        shards,
        mesh=mesh,
        in_specs=(
            P(("groups", "section"), None, None),
            P(("groups", "section"), None, None),
            P(("groups", "section"), None, None),
            P("section", None),
            P("section", None, None),
            P("section", None, None),
            P("section", None, None),
            P(("groups", "section"), None, None),
        ),
        out_specs=(P(("groups", "section"), None, None), P(("groups", "section"), None, None)),
        check_vma=False,
    )
```
